256 devices in a mesh: gx: 16 (over z, x_hi), gy: 16 (over y, x_lo, core).
Axes of the slice: x: 4 (x_hi: 2, x_lo: 2; x = x_hi * 2 + x_lo), y: 4, z: 8, core: 2. Of those that a mesh axis runs over, the one named last changes fastest.
Arguments:
- volume: float32 [64, 32, 128, 128], P(None, 'gx', 'gy'), may hold values from -6 to 6
- cotangent: float32 [64, 32, 128, 128], P(None, 'gx', 'gy'), may hold values from -20 to 20
- weight_one: float32 [27, 4096], replicated, may hold values from -0.17 to 0.16, as said below
- scale_one: float32 [64], replicated, may hold values from 0.001 to 0.016
- weight_two: float32 [27, 4096], replicated, may hold values from -0.17 to 0.16, as said below
- scale_two: float32 [64], replicated, may hold values from 0.001 to 0.016
Outputs:
- input_grad: float32 [64, 32, 128, 128], P(None, 'gx', 'gy')
- kernel_grad_one: float32 [27, 4096], P(None, ('gx', 'gy'))
- scale_grad_one: float32 [64], replicated
- kernel_grad_two: float32 [27, 4096], P(None, ('gx', 'gy'))
- scale_grad_two: float32 [64], replicated
The draws below stay inside these ranges and needn't reach their ends.
Inputs may be any that keep to these rules, and one draw needn't show every extreme that they name: `weight_one`: each entry divided by its output channel's entry of scale_one lies 0.1 to 0.4 away from the nearest integer, between -10.4 and 9.4. `weight_two`: each entry divided by its output channel's entry of scale_two lies 0.1 to 0.4 away from the nearest integer, between -10.4 and 9.4.
All inputs are finite; a program needn't handle non-finite values.
Results may differ from the reference program's by a relative error of at most 0.0003.
Values sent between devices are 32-bit elements; how exact they have to be, the bound alone decides.
No kernel may reach another device: no remote copies, remote signals or barrier semaphores. Data moves between devices by JAX's collectives and lax.ppermute only.
A program may use at most 128 MiB of HBM per device.

```python
import jax
import jax.numpy as jnp
from jax import lax

CH = 64
ZW = 128
NX = 32
NY = 128


def lsq_pair(key, salt):
    base = jax.random.fold_in(key, salt)
    key_scale, key_level, key_frac, key_sign = jax.random.split(base, 4)
    lowest, highest = (0.002, 0.008)
    scales = jnp.exp(jax.random.uniform(key_scale, (CH,), jnp.float32, jnp.log(lowest), jnp.log(highest)))
    levels = jax.random.randint(key_level, (27, CH, CH), -10, 10).astype(jnp.float32)
    fraction = jax.random.uniform(key_frac, (27, CH, CH), jnp.float32, 0.1, 0.4)
    signs = jnp.where(jax.random.bernoulli(key_sign, 0.5, (27, CH, CH)), 1.0, -1.0)
    weight = scales[None, :, None] * (levels + signs * fraction)
    return (weight.reshape(27, CH * CH), scales)


def draw_weight_one(key, part):
    return lsq_pair(key, 11)[0]


def draw_scale_one(key, part):
    return lsq_pair(key, 11)[1]


def draw_weight_two(key, part):
    return lsq_pair(key, 23)[0]


def draw_scale_two(key, part):
    return lsq_pair(key, 23)[1]


def draw_cotangent(key, part):
    key_noise = jax.random.fold_in(jax.random.fold_in(key, 37), 0)
    noise = jax.random.truncated_normal(key_noise, -4.0, 4.0, (CH, NX, NY, ZW), jnp.float32)
    along_x = jnp.arange(NX, dtype=jnp.float32) / max(NX - 1, 1)
    along_y = jnp.arange(NY, dtype=jnp.float32) / max(NY - 1, 1)
    ramp = (along_x[:, None] + along_y[None, :]) / 2.0
    amplitude = 0.6 * 3.0 ** ramp
    return noise * amplitude[None, :, :, None]


def block_levels(key, dims, shards, smallest, top_value):
    def one(dim, shards_of):
        heights = jax.random.uniform(jax.random.fold_in(jax.random.fold_in(key, 6), dim), (shards_of,), jnp.float32, smallest / len(shards), top_value / len(shards))
        return jnp.repeat(jnp.exp(heights), dims[dim] // shards_of).reshape((-1,) + (1,) * (len(dims) - dim - 1))

    level = one(*shards[0])
    for cut in shards[1:]:
        level = level * one(*cut)
    return level


def centred(rng, shape, scale, bound, pieces=(), held_as=jnp.bfloat16):
    array = scale * jax.random.normal(rng, shape, jnp.float32)
    if pieces:
        array = array * block_levels(rng, shape, pieces, -0.22, 0.18)
    return jnp.clip(array, -bound, bound).astype(held_as)


def setup_inputs(seed: int = 0) -> dict:
    seeds = jax.random.split(jax.random.key(seed), 7)
    return {
        "volume": centred(seeds[0], (CH, NX, NY, ZW), 1.0, 6.0, ((1, 16), (2, 16)), jnp.float32),
        "cotangent": draw_cotangent(jax.random.fold_in(seeds[6], 71), 0),
        "weight_one": draw_weight_one(jax.random.fold_in(seeds[6], 71), 0),
        "scale_one": draw_scale_one(jax.random.fold_in(seeds[6], 71), 0),
        "weight_two": draw_weight_two(jax.random.fold_in(seeds[6], 71), 0),
        "scale_two": draw_scale_two(jax.random.fold_in(seeds[6], 71), 0),
    }


CODE_LOW = -8.0
CODE_HIGH = 7.0
REPORT = 2.0 ** (-10)

def quantize(weight, scales):
    channels = scales.shape[0]
    ratios = weight.reshape(27, channels, channels) / scales[None, :, None]
    levels = jnp.clip(jnp.floor(ratios + 0.5), CODE_LOW, CODE_HIGH)
    inside = jnp.logical_and(ratios >= CODE_LOW, ratios <= CODE_HIGH)
    residue = jnp.where(inside, levels - ratios, levels)
    return (levels * scales[None, :, None], inside, residue)

def to_kernel(tap_weights):
    channels = tap_weights.shape[1]
    return tap_weights.reshape(3, 3, 3, channels, channels).transpose(3, 4, 0, 1, 2)

def convolve(signal, kernel):
    return lax.conv_general_dilated(signal[None], kernel, (1, 1, 1), ((1, 1), (1, 1), (1, 1)), dimension_numbers=('NCDHW', 'OIDHW', 'NCDHW'), precision=lax.Precision.HIGHEST)[0]

def forward(signal, taps_first, taps_second):
    hidden = jax.nn.silu(convolve(signal, to_kernel(taps_first)))
    return jax.nn.silu(convolve(hidden, to_kernel(taps_second)))

def reference(volume, cotangent, weight_one, scale_one, weight_two, scale_two):
    taps_one, inside_one, residue_one = quantize(weight_one, scale_one)
    taps_two, inside_two, residue_two = quantize(weight_two, scale_two)
    outcome, pullback = jax.vjp(forward, volume, taps_one, taps_two)
    input_grad, grad_one, grad_two = pullback(cotangent)
    factor = REPORT * (27.0 * CH * CODE_HIGH) ** (-0.5)
    kernel_grad_one = (jnp.where(inside_one, grad_one, 0.0) * REPORT).reshape(27, CH * CH)
    kernel_grad_two = (jnp.where(inside_two, grad_two, 0.0) * REPORT).reshape(27, CH * CH)
    scale_grad_one = factor * lax.optimization_barrier(jnp.sum(grad_one * residue_one, axis=(0, 2)))
    scale_grad_two = factor * lax.optimization_barrier(jnp.sum(grad_two * residue_two, axis=(0, 2)))
    return (input_grad, kernel_grad_one, scale_grad_one, kernel_grad_two, scale_grad_two)
```

```python
import jax
import jax.numpy as jnp
from jax import lax
from jax.sharding import PartitionSpec as P

CODE_LOW = -8.0
CODE_HIGH = 7.0
REPORT = 2.0 ** (-10)


def extended(value, sides, width):
    for axis, dim in sides:
        devices, length = (lax.axis_size(axis), value.shape[dim])
        up = [(i, (i + 1) % devices) for i in range(devices - 1)]
        down = [(j, i) for i, j in up]
        last = lax.slice_in_dim(value, length - width, length, axis=dim)
        leading = lax.slice_in_dim(value, 0, width, axis=dim)
        before = lax.ppermute(last, axis, up)
        after = lax.ppermute(leading, axis, down)
        value = jnp.concatenate([before, value, after], axis=dim)
    return value


def quantize(weight, scales):
    channels = scales.shape[0]
    ratios = weight.reshape(27, channels, channels) / scales[None, :, None]
    levels = jnp.clip(jnp.floor(ratios + 0.5), CODE_LOW, CODE_HIGH)
    inside = jnp.logical_and(ratios >= CODE_LOW, ratios <= CODE_HIGH)
    residue = jnp.where(inside, levels - ratios, levels)
    return (levels * scales[None, :, None], inside, residue)


def to_kernel(tap_weights):
    channels = tap_weights.shape[1]
    return tap_weights.reshape(3, 3, 3, channels, channels).transpose(3, 4, 0, 1, 2)


def convolve(signal, kernel):
    return lax.conv_general_dilated(
        signal[None],
        kernel,
        (1, 1, 1),
        ((0, 0), (0, 0), (1, 1)),
        dimension_numbers=("NCDHW", "OIDHW", "NCDHW"),
        precision=lax.Precision.HIGH,
    )[0]


def transposed(kernel):
    return jnp.flip(kernel, (2, 3, 4)).transpose(1, 0, 2, 3, 4)


def silu_slope(signal):
    sigmoid = jax.nn.sigmoid(signal)
    return sigmoid * (1.0 + signal * (1.0 - sigmoid))


def kernel_grad(signal, deltas, kernel):
    channels = kernel.shape[0]
    outcome, pullback = jax.vjp(lambda taken: convolve(signal, taken), kernel)
    gradient = pullback(deltas)[0]
    return gradient.transpose(2, 3, 4, 0, 1).reshape(27, channels * channels)


def reduce_scatter(grads, partial):
    stack, rows, cols = grads.shape
    nx, ny = lax.axis_size("gx"), lax.axis_size("gy")
    share = cols // (nx * ny)
    blocks = grads.reshape(stack, rows, nx, ny, share).transpose(3, 0, 1, 2, 4)
    blocks = blocks.reshape(ny, stack * rows * nx * share)
    extra = partial.shape[0]
    chunks = jnp.concatenate([blocks, jnp.broadcast_to(partial, (ny, extra))], axis=1)
    summed = lax.all_to_all(chunks, "gy", 0, 0, tiled=True).sum(0)
    head, partial = summed[:-extra], summed[-extra:]
    blocks = head.reshape(stack, rows, nx, share).transpose(2, 0, 1, 3)
    blocks = blocks.reshape(nx, stack * rows * share)
    chunks = jnp.concatenate([blocks, jnp.broadcast_to(partial, (nx, extra))], axis=1)
    summed = lax.all_to_all(chunks, "gx", 0, 0, tiled=True).sum(0)
    return summed[:-extra].reshape(stack, rows, share), summed[-extra:]


def on_device(volume, cotangent, weight_one, scale_one, weight_two, scale_two):
    channels = scale_one.shape[0]
    taps_one, inside_one, residue_one = quantize(weight_one, scale_one)
    taps_two, inside_two, residue_two = quantize(weight_two, scale_two)
    kernel_one = to_kernel(taps_one)
    kernel_two = to_kernel(taps_two)
    padded_in = extended(volume, (("gx", 1), ("gy", 2)), 1)
    first_pre = convolve(padded_in, kernel_one)
    hidden_pad = extended(jax.nn.silu(first_pre), (("gx", 1), ("gy", 2)), 1)
    second_pre = convolve(hidden_pad, kernel_two)
    delta_two = cotangent * silu_slope(second_pre)
    grad_two = kernel_grad(hidden_pad, delta_two, kernel_two)
    delta_pad = extended(delta_two, (("gx", 1), ("gy", 2)), 1)
    delta_one = convolve(delta_pad, transposed(kernel_two)) * silu_slope(first_pre)
    grad_one = kernel_grad(padded_in, delta_one, kernel_one)
    input_pad = extended(delta_one, (("gx", 1), ("gy", 2)), 1)
    input_grad = convolve(input_pad, transposed(kernel_one))
    factor = REPORT * (27.0 * channels * CODE_HIGH) ** (-0.5)
    flat_in_one = inside_one.reshape(27, channels * channels)
    flat_in_two = inside_two.reshape(27, channels * channels)
    partial = jnp.stack(
        [
            jnp.sum(grad_one.reshape(27, channels, channels) * residue_one, axis=(0, 2)),
            jnp.sum(grad_two.reshape(27, channels, channels) * residue_two, axis=(0, 2)),
        ]
    ).reshape(-1)
    grads = jnp.stack([grad_one, grad_two])
    total, scales = reduce_scatter(grads, partial)
    share_cols = total.shape[-1]
    first_col = lax.axis_index(("gx", "gy")) * share_cols
    scale_grad_one = factor * scales[:channels]
    scale_grad_two = factor * scales[channels:]
    kernel_grad_one = jnp.where(
        lax.dynamic_slice_in_dim(flat_in_one, first_col, share_cols, 1), total[0], 0.0
    ) * REPORT
    kernel_grad_two = jnp.where(
        lax.dynamic_slice_in_dim(flat_in_two, first_col, share_cols, 1), total[1], 0.0
    ) * REPORT
    return (input_grad, kernel_grad_one, scale_grad_one, kernel_grad_two, scale_grad_two)


def solution(mesh):
    in_specs = (P(None, "gx", "gy", None), P(None, "gx", "gy", None), P(), P(), P(), P())
    out_specs = (P(None, "gx", "gy", None), P(None, ("gx", "gy")), P(), P(None, ("gx", "gy")), P())
    return jax.shard_map(
        on_device, mesh=mesh, in_specs=in_specs, out_specs=out_specs, check_vma=False
    )
```

```python
import jax
import jax.numpy as jnp
from jax import lax
from jax.sharding import PartitionSpec as P

CODE_LOW = -8.0
CODE_HIGH = 7.0
REPORT = 2.0 ** (-10)


def extended(value, sides, width):
    for axis, dim in sides:
        devices, length = (lax.axis_size(axis), value.shape[dim])
        up = [(i, (i + 1) % devices) for i in range(devices - 1)]
        down = [(j, i) for i, j in up]
        last = lax.slice_in_dim(value, length - width, length, axis=dim)
        leading = lax.slice_in_dim(value, 0, width, axis=dim)
        before = lax.ppermute(last, axis, up)
        after = lax.ppermute(leading, axis, down)
        value = jnp.concatenate([before, value, after], axis=dim)
    return value


def quantize(weight, scales):
    channels = scales.shape[0]
    ratios = weight.reshape(27, channels, channels) / scales[None, :, None]
    levels = jnp.clip(jnp.floor(ratios + 0.5), CODE_LOW, CODE_HIGH)
    inside = jnp.logical_and(ratios >= CODE_LOW, ratios <= CODE_HIGH)
    residue = jnp.where(inside, levels - ratios, levels)
    return (levels * scales[None, :, None], inside, residue)


def to_kernel(tap_weights):
    channels = tap_weights.shape[1]
    return tap_weights.reshape(3, 3, 3, channels, channels).transpose(3, 4, 0, 1, 2)


def convolve(signal, kernel):
    return lax.conv_general_dilated(
        signal[None],
        kernel,
        (1, 1, 1),
        ((0, 0), (0, 0), (1, 1)),
        dimension_numbers=("NCDHW", "OIDHW", "NCDHW"),
        precision=lax.Precision.HIGH,
    )[0]


def transposed(kernel):
    return jnp.flip(kernel, (2, 3, 4)).transpose(1, 0, 2, 3, 4)


def silu_slope(signal):
    sigmoid = jax.nn.sigmoid(signal)
    return sigmoid * (1.0 + signal * (1.0 - sigmoid))


def kernel_grad(signal, deltas, kernel):
    channels = kernel.shape[0]
    rows, cols, depth = deltas.shape[1:]
    padded = jnp.pad(signal, ((0, 0), (0, 0), (0, 0), (1, 1)))
    shifted = jnp.stack(
        [
            padded[:, a : a + rows, b : b + cols, c : c + depth]
            for a in range(3)
            for b in range(3)
            for c in range(3)
        ]
    )
    gradient = jnp.einsum(
        "op,tip->toi",
        deltas.reshape(channels, -1),
        shifted.reshape(27, channels, -1),
        precision=lax.Precision.HIGH,
    )
    return gradient.reshape(27, channels * channels)


def reduce_scatter(grads, partial):
    stack, rows, cols = grads.shape
    nx, ny = lax.axis_size("gx"), lax.axis_size("gy")
    share = cols // (nx * ny)
    blocks = grads.reshape(stack, rows, nx, ny, share).transpose(3, 0, 1, 2, 4)
    blocks = blocks.reshape(ny, stack * rows * nx * share)
    extra = partial.shape[0]
    chunks = jnp.concatenate([blocks, jnp.broadcast_to(partial, (ny, extra))], axis=1)
    summed = lax.all_to_all(chunks, "gy", 0, 0, tiled=True).sum(0)
    head, partial = summed[:-extra], summed[-extra:]
    blocks = head.reshape(stack, rows, nx, share).transpose(2, 0, 1, 3)
    blocks = blocks.reshape(nx, stack * rows * share)
    chunks = jnp.concatenate([blocks, jnp.broadcast_to(partial, (nx, extra))], axis=1)
    summed = lax.all_to_all(chunks, "gx", 0, 0, tiled=True).sum(0)
    return summed[:-extra].reshape(stack, rows, share), summed[-extra:]


def on_device(volume, cotangent, weight_one, scale_one, weight_two, scale_two):
    channels = scale_one.shape[0]
    taps_one, inside_one, residue_one = quantize(weight_one, scale_one)
    taps_two, inside_two, residue_two = quantize(weight_two, scale_two)
    kernel_one = to_kernel(taps_one)
    kernel_two = to_kernel(taps_two)
    padded_in = extended(volume, (("gx", 1), ("gy", 2)), 1)
    first_pre = convolve(padded_in, kernel_one)
    hidden_pad = extended(jax.nn.silu(first_pre), (("gx", 1), ("gy", 2)), 1)
    second_pre = convolve(hidden_pad, kernel_two)
    delta_two = cotangent * silu_slope(second_pre)
    grad_two = kernel_grad(hidden_pad, delta_two, kernel_two)
    delta_pad = extended(delta_two, (("gx", 1), ("gy", 2)), 1)
    delta_one = convolve(delta_pad, transposed(kernel_two)) * silu_slope(first_pre)
    grad_one = kernel_grad(padded_in, delta_one, kernel_one)
    input_pad = extended(delta_one, (("gx", 1), ("gy", 2)), 1)
    input_grad = convolve(input_pad, transposed(kernel_one))
    factor = REPORT * (27.0 * channels * CODE_HIGH) ** (-0.5)
    flat_in_one = inside_one.reshape(27, channels * channels)
    flat_in_two = inside_two.reshape(27, channels * channels)
    partial = jnp.stack(
        [
            jnp.sum(grad_one.reshape(27, channels, channels) * residue_one, axis=(0, 2)),
            jnp.sum(grad_two.reshape(27, channels, channels) * residue_two, axis=(0, 2)),
        ]
    ).reshape(-1)
    grads = jnp.stack([grad_one, grad_two])
    total, scales = reduce_scatter(grads, partial)
    share_cols = total.shape[-1]
    first_col = lax.axis_index(("gx", "gy")) * share_cols
    scale_grad_one = factor * scales[:channels]
    scale_grad_two = factor * scales[channels:]
    kernel_grad_one = jnp.where(
        lax.dynamic_slice_in_dim(flat_in_one, first_col, share_cols, 1), total[0], 0.0
    ) * REPORT
    kernel_grad_two = jnp.where(
        lax.dynamic_slice_in_dim(flat_in_two, first_col, share_cols, 1), total[1], 0.0
    ) * REPORT
    return (input_grad, kernel_grad_one, scale_grad_one, kernel_grad_two, scale_grad_two)


def solution(mesh):
    in_specs = (P(None, "gx", "gy", None), P(None, "gx", "gy", None), P(), P(), P(), P())
    out_specs = (P(None, "gx", "gy", None), P(None, ("gx", "gy")), P(), P(None, ("gx", "gy")), P())
    return jax.shard_map(
        on_device, mesh=mesh, in_specs=in_specs, out_specs=out_specs, check_vma=False
    )
```

```python
import jax
import jax.numpy as jnp
from jax import lax
from jax.sharding import PartitionSpec as P

CODE_LOW = -8.0
CODE_HIGH = 7.0
REPORT = 2.0 ** (-10)


def extended(value, sides, width):
    for axis, dim in sides:
        devices, length = (lax.axis_size(axis), value.shape[dim])
        up = [(i, (i + 1) % devices) for i in range(devices - 1)]
        down = [(j, i) for i, j in up]
        last = lax.slice_in_dim(value, length - width, length, axis=dim)
        leading = lax.slice_in_dim(value, 0, width, axis=dim)
        before = lax.ppermute(last, axis, up)
        after = lax.ppermute(leading, axis, down)
        value = jnp.concatenate([before, value, after], axis=dim)
    return value


def quantize(weight, scales):
    channels = scales.shape[0]
    ratios = weight.reshape(27, channels, channels) / scales[None, :, None]
    levels = jnp.clip(jnp.floor(ratios + 0.5), CODE_LOW, CODE_HIGH)
    inside = jnp.logical_and(ratios >= CODE_LOW, ratios <= CODE_HIGH)
    residue = jnp.where(inside, levels - ratios, levels)
    return (levels * scales[None, :, None], inside, residue)


def to_kernel(tap_weights):
    channels = tap_weights.shape[1]
    return tap_weights.reshape(3, 3, 3, channels, channels).transpose(3, 4, 0, 1, 2)


def convolve(signal, kernel):
    return lax.conv_general_dilated(
        signal[None],
        kernel,
        (1, 1, 1),
        ((0, 0), (0, 0), (1, 1)),
        dimension_numbers=("NCDHW", "OIDHW", "NCDHW"),
        precision=lax.Precision.HIGH,
    )[0]


def transposed(kernel):
    return jnp.flip(kernel, (2, 3, 4)).transpose(1, 0, 2, 3, 4)


def silu_slope(signal):
    sigmoid = jax.nn.sigmoid(signal)
    return sigmoid * (1.0 + signal * (1.0 - sigmoid))


def kernel_grad(signal, deltas, kernel):
    channels = kernel.shape[0]
    rows, cols, depth = deltas.shape[1:]
    padded = jnp.pad(signal, ((0, 0), (0, 0), (0, 0), (1, 1)))
    shifted = jnp.stack(
        [
            padded[:, a : a + rows, b : b + cols, c : c + depth]
            for a in range(3)
            for b in range(3)
            for c in range(3)
        ]
    )
    return jnp.einsum(
        "op,tip->oti",
        deltas.reshape(channels, -1),
        shifted.reshape(27, channels, -1),
        precision=lax.Precision.HIGH,
    )


def reduce_scatter(grads, partial):
    channels, stack, taps, inputs = grads.shape
    nx, ny = lax.axis_size("gx"), lax.axis_size("gy")
    share = channels * inputs // (nx * ny)
    per, split = channels // nx, inputs // share
    extra = partial.shape[0]
    blocks = grads.reshape(nx, -1)
    chunks = jnp.concatenate([blocks, jnp.broadcast_to(partial, (nx, extra))], axis=1)
    summed = lax.all_to_all(chunks, "gx", 0, 0, tiled=True).sum(0)
    head, partial = summed[:-extra], summed[-extra:]
    blocks = head.reshape(per, stack, taps, split, share).transpose(0, 3, 1, 2, 4)
    blocks = blocks.reshape(ny, stack * taps * share)
    chunks = jnp.concatenate([blocks, jnp.broadcast_to(partial, (ny, extra))], axis=1)
    summed = lax.all_to_all(chunks, "gy", 0, 0, tiled=True).sum(0)
    return summed[:-extra].reshape(stack, taps, share), summed[-extra:]


def on_device(volume, cotangent, weight_one, scale_one, weight_two, scale_two):
    channels = scale_one.shape[0]
    taps_one, inside_one, residue_one = quantize(weight_one, scale_one)
    taps_two, inside_two, residue_two = quantize(weight_two, scale_two)
    kernel_one = to_kernel(taps_one)
    kernel_two = to_kernel(taps_two)
    padded_in = extended(volume, (("gx", 1), ("gy", 2)), 1)
    first_pre = convolve(padded_in, kernel_one)
    hidden_pad = extended(jax.nn.silu(first_pre), (("gx", 1), ("gy", 2)), 1)
    second_pre = convolve(hidden_pad, kernel_two)
    delta_two = cotangent * silu_slope(second_pre)
    grad_two = kernel_grad(hidden_pad, delta_two, kernel_two)
    delta_pad = extended(delta_two, (("gx", 1), ("gy", 2)), 1)
    delta_one = convolve(delta_pad, transposed(kernel_two)) * silu_slope(first_pre)
    grad_one = kernel_grad(padded_in, delta_one, kernel_one)
    input_pad = extended(delta_one, (("gx", 1), ("gy", 2)), 1)
    input_grad = convolve(input_pad, transposed(kernel_one))
    factor = REPORT * (27.0 * channels * CODE_HIGH) ** (-0.5)
    flat_in_one = inside_one.reshape(27, channels * channels)
    flat_in_two = inside_two.reshape(27, channels * channels)
    partial = jnp.stack(
        [
            jnp.sum(grad_one * residue_one.transpose(1, 0, 2), axis=(1, 2)),
            jnp.sum(grad_two * residue_two.transpose(1, 0, 2), axis=(1, 2)),
        ]
    ).reshape(-1)
    grads = jnp.stack([grad_one, grad_two], axis=1)
    total, scales = reduce_scatter(grads, partial)
    share_cols = total.shape[-1]
    first_col = lax.axis_index(("gx", "gy")) * share_cols
    scale_grad_one = factor * scales[:channels]
    scale_grad_two = factor * scales[channels:]
    kernel_grad_one = jnp.where(
        lax.dynamic_slice_in_dim(flat_in_one, first_col, share_cols, 1), total[0], 0.0
    ) * REPORT
    kernel_grad_two = jnp.where(
        lax.dynamic_slice_in_dim(flat_in_two, first_col, share_cols, 1), total[1], 0.0
    ) * REPORT
    return (input_grad, kernel_grad_one, scale_grad_one, kernel_grad_two, scale_grad_two)


def solution(mesh):
    in_specs = (P(None, "gx", "gy", None), P(None, "gx", "gy", None), P(), P(), P(), P())
    out_specs = (P(None, "gx", "gy", None), P(None, ("gx", "gy")), P(), P(None, ("gx", "gy")), P())
    return jax.shard_map(
        on_device, mesh=mesh, in_specs=in_specs, out_specs=out_specs, check_vma=False
    )
```

```python
import jax
import jax.numpy as jnp
from jax import lax
from jax.sharding import PartitionSpec as P

CODE_LOW = -8.0
CODE_HIGH = 7.0
REPORT = 2.0 ** (-10)


def extended(value, sides, width):
    for axis, dim in sides:
        devices, length = (lax.axis_size(axis), value.shape[dim])
        up = [(i, (i + 1) % devices) for i in range(devices - 1)]
        down = [(j, i) for i, j in up]
        last = lax.slice_in_dim(value, length - width, length, axis=dim)
        leading = lax.slice_in_dim(value, 0, width, axis=dim)
        before = lax.ppermute(last, axis, up)
        after = lax.ppermute(leading, axis, down)
        value = jnp.concatenate([before, value, after], axis=dim)
    return value


def quantize(weight, scales):
    channels = scales.shape[0]
    ratios = weight.reshape(27, channels, channels) / scales[None, :, None]
    levels = jnp.clip(jnp.floor(ratios + 0.5), CODE_LOW, CODE_HIGH)
    inside = jnp.logical_and(ratios >= CODE_LOW, ratios <= CODE_HIGH)
    residue = jnp.where(inside, levels - ratios, levels)
    return (levels * scales[None, :, None], inside, residue, levels)


def to_kernel(tap_weights):
    channels = tap_weights.shape[1]
    return tap_weights.reshape(3, 3, 3, channels, channels).transpose(3, 4, 0, 1, 2)


def convolve(signal, kernel):
    return lax.conv_general_dilated(
        signal[None],
        kernel,
        (1, 1, 1),
        ((0, 0), (0, 0), (1, 1)),
        dimension_numbers=("NCDHW", "OIDHW", "NCDHW"),
        precision=lax.Precision.HIGH,
    )[0]


def split_conv(signal, levels):
    head = lax.reduce_precision(signal, exponent_bits=8, mantissa_bits=7)
    parts = jnp.concatenate([head, signal - head]).astype(jnp.bfloat16)
    kernel = levels.astype(jnp.bfloat16)
    return lax.conv_general_dilated(
        parts[None],
        jnp.concatenate([kernel, kernel], axis=1),
        (1, 1, 1),
        ((0, 0), (0, 0), (1, 1)),
        dimension_numbers=("NCDHW", "OIDHW", "NCDHW"),
        preferred_element_type=jnp.float32,
    )[0]


def transposed(kernel):
    return jnp.flip(kernel, (2, 3, 4)).transpose(1, 0, 2, 3, 4)


def silu_slope(signal):
    sigmoid = jax.nn.sigmoid(signal)
    return sigmoid * (1.0 + signal * (1.0 - sigmoid))


def kernel_grad(signal, deltas, kernel):
    channels = kernel.shape[0]
    rows, cols, depth = deltas.shape[1:]
    padded = jnp.pad(signal, ((0, 0), (0, 0), (0, 0), (1, 1)))
    shifted = jnp.stack(
        [
            padded[:, a : a + rows, b : b + cols, c : c + depth]
            for a in range(3)
            for b in range(3)
            for c in range(3)
        ]
    )
    return jnp.einsum(
        "op,tip->oti",
        deltas.reshape(channels, -1),
        shifted.reshape(27, channels, -1),
        precision=lax.Precision.HIGH,
    )


def reduce_scatter(grads, partial):
    channels, stack, taps, inputs = grads.shape
    nx, ny = lax.axis_size("gx"), lax.axis_size("gy")
    share = channels * inputs // (nx * ny)
    per, split = channels // nx, inputs // share
    extra = partial.shape[0]
    blocks = grads.reshape(nx, -1)
    chunks = jnp.concatenate([blocks, jnp.broadcast_to(partial, (nx, extra))], axis=1)
    summed = lax.all_to_all(chunks, "gx", 0, 0, tiled=True).sum(0)
    head, partial = summed[:-extra], summed[-extra:]
    blocks = head.reshape(per, stack, taps, split, share).transpose(0, 3, 1, 2, 4)
    blocks = blocks.reshape(ny, stack * taps * share)
    chunks = jnp.concatenate([blocks, jnp.broadcast_to(partial, (ny, extra))], axis=1)
    summed = lax.all_to_all(chunks, "gy", 0, 0, tiled=True).sum(0)
    return summed[:-extra].reshape(stack, taps, share), summed[-extra:]


def on_device(volume, cotangent, weight_one, scale_one, weight_two, scale_two):
    channels = scale_one.shape[0]
    _, inside_one, residue_one, level_one = quantize(weight_one, scale_one)
    _, inside_two, residue_two, level_two = quantize(weight_two, scale_two)
    kernel_one = to_kernel(level_one)
    kernel_two = to_kernel(level_two)
    step_one = scale_one[:, None, None, None]
    step_two = scale_two[:, None, None, None]
    padded_in = extended(volume, (("gx", 1), ("gy", 2)), 1)
    first_pre = step_one * split_conv(padded_in, kernel_one)
    hidden_pad = extended(jax.nn.silu(first_pre), (("gx", 1), ("gy", 2)), 1)
    second_pre = step_two * split_conv(hidden_pad, kernel_two)
    delta_two = cotangent * silu_slope(second_pre)
    grad_two = kernel_grad(hidden_pad, delta_two, kernel_two)
    delta_pad = extended(delta_two, (("gx", 1), ("gy", 2)), 1)
    delta_one = split_conv(delta_pad * step_two, transposed(kernel_two)) * silu_slope(first_pre)
    grad_one = kernel_grad(padded_in, delta_one, kernel_one)
    input_pad = extended(delta_one, (("gx", 1), ("gy", 2)), 1)
    input_grad = split_conv(input_pad * step_one, transposed(kernel_one))
    factor = REPORT * (27.0 * channels * CODE_HIGH) ** (-0.5)
    flat_in_one = inside_one.reshape(27, channels * channels)
    flat_in_two = inside_two.reshape(27, channels * channels)
    partial = jnp.stack(
        [
            jnp.sum(grad_one * residue_one.transpose(1, 0, 2), axis=(1, 2)),
            jnp.sum(grad_two * residue_two.transpose(1, 0, 2), axis=(1, 2)),
        ]
    ).reshape(-1)
    grads = jnp.stack([grad_one, grad_two], axis=1)
    total, scales = reduce_scatter(grads, partial)
    share_cols = total.shape[-1]
    first_col = lax.axis_index(("gx", "gy")) * share_cols
    scale_grad_one = factor * scales[:channels]
    scale_grad_two = factor * scales[channels:]
    kernel_grad_one = jnp.where(
        lax.dynamic_slice_in_dim(flat_in_one, first_col, share_cols, 1), total[0], 0.0
    ) * REPORT
    kernel_grad_two = jnp.where(
        lax.dynamic_slice_in_dim(flat_in_two, first_col, share_cols, 1), total[1], 0.0
    ) * REPORT
    return (input_grad, kernel_grad_one, scale_grad_one, kernel_grad_two, scale_grad_two)


def solution(mesh):
    in_specs = (P(None, "gx", "gy", None), P(None, "gx", "gy", None), P(), P(), P(), P())
    out_specs = (P(None, "gx", "gy", None), P(None, ("gx", "gy")), P(), P(None, ("gx", "gy")), P())
    return jax.shard_map(
        on_device, mesh=mesh, in_specs=in_specs, out_specs=out_specs, check_vma=False
    )
```
